128 devices in a mesh: gx: 16 (over x, y), gy: 8 (over z, core).
Axes of the slice: x: 4, y: 4, z: 4, core: 2. Of those that a mesh axis runs over, the one named last changes fastest.
Arguments:
- fields: bfloat16 [10, 32, 1024, 1024], P(None, None, 'gx', 'gy'), as said below
- dense_list: int32 [8, 16, 20], replicated, may hold values from -1 to 63, as said below
- filter_device: int32 [8, 16, 20], replicated, may hold values from -1 to 15, as said below
- pencil_order: int32 [32], replicated, may hold values from 0 to 31, each once
Outputs:
- tile_stats: float32 [1024, 2048], P(('gx', 'gy'))
- coarse_closure: float32 [32, 1024], P('gy')
The draws below stay inside these ranges and needn't reach their ends.
Inputs may be any that keep to these rules, and one draw needn't show every extreme that they name: `dense_list`: row [gy, gx] lists distinct local tile indices of device (gx, gy), its listed entries first and -1 after them; in every gy row the busiest device lists 20 tiles and some list only a few. `filter_device`: -1 exactly where dense_list is -1; within a gy row each gx index receives exactly 8 listed tiles and at most 2 from any one listing device, and that most is met. `fields`: channel 0 lies between 0.05 and 0.6; channels 8 and 9 are positive.
All inputs are finite; a program needn't handle non-finite values.
Results may differ from the reference program's by a relative error of at most 0.0003.
Values may be sent and summed in bfloat16 or wider, within the bound.
No kernel may reach another device: no remote copies, remote signals or barrier semaphores. Data moves between devices by JAX's collectives and lax.ppermute only.
A program may use at most 192 MiB of HBM per device.

```python
import jax
import jax.numpy as jnp
from jax import lax

TE = 16
HW = 4
CAP = 2
TXD = 4
TYD = 8
TILE_DEV = 64
NX = 1024
NY = 1024
NZ = 32
DLIST = 20
DMEAN = 8
CXN = 32
NPEN = 32
SUB = 64
LSTAT = 2048
N_GX = 16
N_GY = 8


def tile_plan(base_key):
    quarter = N_GX // 4
    heavy_load = CAP - 1
    source_index = jnp.arange(N_GX, dtype=jnp.int32)
    source_load = jnp.where(source_index < quarter, heavy_load, jnp.where(source_index < 2 * quarter, heavy_load // 2, 0)).astype(jnp.int32)

    def one_group(group_key):
        key_set = jax.random.split(group_key, 3 + N_GX)
        row_perm = jax.random.permutation(key_set[0], N_GX)
        column_perm = jax.random.permutation(key_set[1], N_GX)
        extra_ones = (jax.random.permutation(key_set[2], N_GX) < quarter).astype(jnp.int32)
        index_i = jnp.arange(N_GX, dtype=jnp.int32)[:, None]
        index_j = jnp.arange(N_GX, dtype=jnp.int32)[None, :]
        base_counts = source_load[:, None] + extra_ones[(index_i + index_j) % N_GX]
        counts = base_counts[row_perm][:, column_perm]

        def one_source(source_key, count_row):
            sub_keys = jax.random.split(source_key, 2)
            candidate = jnp.arange(N_GX * CAP, dtype=jnp.int32)
            target = candidate // CAP
            is_taken = candidate % CAP < count_row[target]
            ranking = jnp.where(is_taken, 0, N_GX * CAP) + jax.random.permutation(sub_keys[0], N_GX * CAP).astype(jnp.int32)
            chosen_order = jnp.argsort(ranking)[:DLIST]
            is_valid = is_taken[chosen_order]
            targets = jnp.where(is_valid, target[chosen_order], -1)
            tile_ids = jnp.where(is_valid, jax.random.permutation(sub_keys[1], TILE_DEV)[:DLIST].astype(jnp.int32), -1)
            return (tile_ids, targets)
        return jax.vmap(one_source)(key_set[3:], counts)
    group_keys = jax.random.split(base_key, N_GY)
    tile_ids, targets = jax.vmap(one_group)(group_keys)
    return (tile_ids.astype(jnp.int32), targets.astype(jnp.int32))


def draw_dense_list(key, part):
    return tile_plan(jax.random.fold_in(key, 11))[0]


def draw_filter_device(key, part):
    return tile_plan(jax.random.fold_in(key, 11))[1]


def draw_fields(key, part):
    key_set = jax.random.split(key, 16)
    grid_shape = (NZ, NX, NY)
    tile_shape = (NZ // TE, NX // TE, NY // TE)

    def spread_tiles(values):
        return jnp.repeat(jnp.repeat(jnp.repeat(values, TE, 0), TE, 1), TE, 2)
    solid = jax.random.uniform(key_set[0], grid_shape, jnp.float32, 0.05, 0.6)
    strength = spread_tiles(jnp.exp(jax.random.uniform(key_set[1], tile_shape, jnp.float32, jnp.log(0.25), jnp.log(4.0))))

    def noise(number):
        return jax.random.normal(key_set[number], grid_shape, jnp.float32)
    signs = (0.5, 1.0, -1.5)
    deviation = solid - 0.325
    channels = [solid.astype(jnp.bfloat16)]
    gas_speed = [8.0 * signs[direction] * strength * deviation + noise(2 + direction) for direction in range(3)]
    channels = channels + [speed.astype(jnp.bfloat16) for speed in gas_speed]
    channels = channels + [(0.5 * gas_speed[direction] + 0.5 * noise(5 + direction)).astype(jnp.bfloat16) for direction in range(3)]
    channels.append((4.0 * strength * deviation + noise(8)).astype(jnp.bfloat16))
    granular = jnp.exp(jax.random.uniform(key_set[9], grid_shape, jnp.float32, jnp.log(0.1), 0.0))
    channels.append(granular.astype(jnp.bfloat16))
    friction = jnp.exp(jax.random.uniform(key_set[10], grid_shape, jnp.float32, 0.0, jnp.log(10.0))) * solid / 0.3
    channels.append(friction.astype(jnp.bfloat16))
    return jnp.stack(channels, axis=0)


def setup_inputs(seed: int = 0) -> dict:
    splits = jax.random.split(jax.random.key(seed), 5)
    return {
        "fields": draw_fields(jax.random.fold_in(splits[4], 71), 0),
        "dense_list": draw_dense_list(jax.random.fold_in(splits[4], 71), 0),
        "filter_device": draw_filter_device(jax.random.fold_in(splits[4], 71), 0),
        "pencil_order": jax.random.permutation(splits[3], NPEN).astype(jnp.int32),
    }


def prefix_sums(values, axis):
    running = jnp.cumsum(values, axis=axis)
    lead_shape = list(values.shape)
    lead_shape[axis] = 1
    return jnp.concatenate([jnp.zeros(lead_shape, values.dtype), running], axis=axis)


def window_cut(sums, axis, half_width):
    upper = lax.slice_in_dim(sums, HW + half_width + 1, HW + half_width + 1 + TE, axis=axis)
    lower = lax.slice_in_dim(sums, HW - half_width, HW - half_width + TE, axis=axis)
    return (upper - lower) / (2 * half_width + 1)


def closure_terms(smoothed):
    solid_mean = smoothed[0]
    components = []
    for direction in range(3):
        components.append(smoothed[6 + direction] / solid_mean - smoothed[1 + direction])
    for direction in range(3):
        components.append(smoothed[14 + direction] - smoothed[5] * (smoothed[6 + direction] - smoothed[9 + direction]) / solid_mean)
    components.append(smoothed[12] / solid_mean)
    components.append(smoothed[13] / solid_mean - smoothed[4])
    return jnp.stack(components, axis=0)


def reference(fields, dense_list, filter_device, pencil_order):
    group_no = lax.broadcasted_iota(jnp.int32, dense_list.shape, 0)
    source_no = lax.broadcasted_iota(jnp.int32, dense_list.shape, 1)
    entry_no = lax.broadcasted_iota(jnp.int32, dense_list.shape, 2)
    ranking = ((filter_device * N_GY + group_no) * N_GX + source_no) * DLIST + entry_no
    ranking = jnp.where(filter_device >= 0, ranking, N_GX * N_GY * N_GX * DLIST)
    picked = jnp.argsort(ranking.reshape(-1))[: N_GX * N_GY * DMEAN]
    tile_ids = dense_list.reshape(-1)[picked]
    depth_at = tile_ids // (TXD * TYD)
    column_at = source_no.reshape(-1)[picked] * TXD + (tile_ids // TYD) % TXD
    row_at = group_no.reshape(-1)[picked] * TYD + tile_ids % TYD
    offsets = jnp.arange(TE + 2 * HW, dtype=jnp.int32) - HW

    def extract(depth_one, column_one, row_one):
        z_index = (depth_one * TE + offsets) % NZ
        x_index = (column_one * TE + offsets) % NX
        y_index = (row_one * TE + offsets) % NY
        return fields[:, z_index[:, None, None], x_index[None, :, None], y_index[None, None, :]]

    def block_stats(positions):
        cell_values = jax.vmap(extract)(positions[0], positions[1], positions[2]).astype(jnp.float32)
        tile_count = cell_values.shape[0]
        solid = cell_values[:, 0]
        gas_speed = [cell_values[:, 1 + direction] for direction in range(3)]
        grain_speed = [cell_values[:, 4 + direction] for direction in range(3)]
        pressure = cell_values[:, 7]
        granular = cell_values[:, 8]
        friction = cell_values[:, 9]
        quantity_list = [solid] + gas_speed + [pressure, friction]
        quantity_list = quantity_list + [solid * speed for speed in gas_speed]
        quantity_list = quantity_list + [solid * speed for speed in grain_speed]
        quantity_list = quantity_list + [solid * granular, solid * pressure]
        quantity_list = quantity_list + [friction * (gas_speed[direction] - grain_speed[direction]) for direction in range(3)]
        stacked = jnp.stack(quantity_list, axis=0)
        sub_edge = TE // 4
        per_width = []
        for half_width in range(1, HW + 1):
            smoothed = stacked
            for axis in (2, 3, 4):
                smoothed = window_cut(prefix_sums(smoothed, axis), axis, half_width)
            closure = closure_terms(smoothed).reshape(8, tile_count, sub_edge, 4, sub_edge, 4, sub_edge, 4)
            per_width.append(jnp.mean(closure, axis=(3, 5, 7)).reshape(8, tile_count, SUB))
        result = jnp.stack(per_width, axis=0)
        return jnp.transpose(result, (2, 0, 1, 3)).reshape(tile_count, LSTAT)

    positions = (depth_at.reshape(N_GX * N_GY, DMEAN), column_at.reshape(N_GX * N_GY, DMEAN), row_at.reshape(N_GX * N_GY, DMEAN))
    tile_stats = lax.map(block_stats, positions).reshape(N_GX * N_GY * DMEAN, LSTAT)
    tile_means = jnp.mean(tile_stats.reshape(N_GX * N_GY * DMEAN, HW * 8, SUB), axis=2)
    cell_no = (row_at // 2) * CXN + column_at // 2
    cell_sums = jax.ops.segment_sum(tile_means, cell_no, num_segments=NPEN * CXN)
    counts = jax.ops.segment_sum(jnp.ones_like(tile_means[:, 0]), cell_no, num_segments=NPEN * CXN)
    averaged = cell_sums / jnp.maximum(counts, 1.0)[:, None]
    pencil_grid = averaged.reshape(NPEN, CXN * HW * 8)
    return tile_stats, pencil_grid[pencil_order]
```

```python
import jax
import jax.numpy as jnp
from jax import lax
from jax.sharding import PartitionSpec as P

TE = 16
HW = 4
CAP = 2


HIGHEST = lax.Precision.HIGHEST


def with_halo(block, sides, width):
    for axis, dim in sides:
        count = lax.axis_size(axis)
        forward = [(i, i + 1) for i in range(count - 1)]
        forward.append((count - 1, 0))
        backward = [(target, source) for source, target in forward]
        low = lax.ppermute(
            lax.slice_in_dim(block, block.shape[dim] - width, None, axis=dim), axis, forward
        )
        high = lax.ppermute(lax.slice_in_dim(block, 0, width, axis=dim), axis, backward)
        block = jnp.concatenate([low, block, high], axis=dim)
    return block


def band_matrix(half_width):
    span = TE + 2 * HW
    row_index = lax.broadcasted_iota(jnp.int32, (TE, span), 0)
    column_index = lax.broadcasted_iota(jnp.int32, (TE, span), 1)
    inside = jnp.abs(column_index - row_index - HW) <= half_width
    return jnp.where(inside, 1.0 / (2 * half_width + 1), 0.0).astype(jnp.float32)


def plane_matrix(half_width):
    span = TE + 2 * HW
    weights = band_matrix(half_width)
    return jnp.einsum("ax,by->xyab", weights, weights, precision=HIGHEST).reshape(
        span * span, TE * TE
    )


def box_band(columns, half_width):
    along_z = jnp.einsum("az,qtzp->qtap", band_matrix(half_width), columns, precision=HIGHEST)
    return jnp.einsum("qtap,pc->qtac", along_z, plane_matrix(half_width), precision=HIGHEST)


def quantities(tiles):
    span = TE + 2 * HW
    tile_count = tiles.shape[0]
    cell_values = tiles.astype(jnp.float32).reshape(tile_count, tiles.shape[1], span, span * span)
    solid = cell_values[:, 0]
    gas_speed = [cell_values[:, 1 + direction] for direction in range(3)]
    grain_speed = [cell_values[:, 4 + direction] for direction in range(3)]
    pressure = cell_values[:, 7]
    granular = cell_values[:, 8]
    friction = cell_values[:, 9]
    quantity_list = [solid] + gas_speed + [pressure, friction]
    quantity_list = quantity_list + [solid * speed for speed in gas_speed]
    quantity_list = quantity_list + [solid * speed for speed in grain_speed]
    quantity_list = quantity_list + [solid * granular, solid * pressure]
    quantity_list = quantity_list + [
        friction * (gas_speed[direction] - grain_speed[direction]) for direction in range(3)
    ]
    return jnp.stack(quantity_list, axis=0)


def block_matrix():
    sub_edge = TE // 4
    plane_index = lax.broadcasted_iota(jnp.int32, (TE * TE, sub_edge * sub_edge), 0)
    block_index = lax.broadcasted_iota(jnp.int32, (TE * TE, sub_edge * sub_edge), 1)
    block_of = plane_index // TE // 4 * sub_edge + plane_index % TE // 4
    return jnp.where(block_of == block_index, 1.0 / 16.0, 0.0).astype(jnp.float32)


def closure_blocks(smoothed):
    solid_mean = smoothed[0]
    components = []
    for direction in range(3):
        components.append(smoothed[6 + direction] / solid_mean - smoothed[1 + direction])
    for direction in range(3):
        components.append(
            smoothed[14 + direction]
            - smoothed[5] * (smoothed[6 + direction] - smoothed[9 + direction]) / solid_mean
        )
    components.append(smoothed[12] / solid_mean)
    components.append(smoothed[13] / solid_mean - smoothed[4])
    sub_edge = TE // 4
    stacked = jnp.stack(components, axis=0)
    tile_count = stacked.shape[1]
    depth_mean = jnp.mean(stacked.reshape(8, tile_count, sub_edge, 4, TE * TE), axis=3)
    blocks = jnp.einsum("ktzp,pc->ktzc", depth_mean, block_matrix(), precision=HIGHEST)
    return blocks.reshape(8, tile_count, sub_edge**3)


def tile_statistics(tiles):
    total_tiles = tiles.shape[0]
    columns = quantities(tiles)
    results = []
    for half_width in range(1, HW + 1):
        results.append(closure_blocks(box_band(columns, half_width)))
    mapped = jnp.stack(results, axis=0)
    return jnp.transpose(mapped, (2, 0, 1, 3)).reshape(total_tiles, HW * 8 * (TE // 4) ** 3)


def cut_tiles(padded, tile_ids, across_x, across_y):
    span = TE + 2 * HW
    depth_at = tile_ids // (across_x * across_y)
    column_at = tile_ids // across_y % across_x
    row_at = tile_ids % across_y

    def single_tile(depth_one, column_one, row_one):
        return lax.dynamic_slice(
            padded,
            (jnp.int32(0), depth_one * TE, column_one * TE, row_one * TE),
            (padded.shape[0], span, span, span),
        )

    pieces = jax.vmap(single_tile)(depth_at, column_at, row_at)
    return pieces.reshape(tile_ids.shape[0], padded.shape[0], span * span * span)


def shards(fields, dense_list, filter_device, pencil_order):
    groups_x = lax.axis_size("gx")
    groups_y = lax.axis_size("gy")
    self_column = lax.axis_index("gx")
    self_row = lax.axis_index("gy")
    across_x = fields.shape[2] // TE
    across_y = fields.shape[3] // TE
    list_length = dense_list.shape[2]
    per_filter = groups_x // 4 * (CAP + (CAP - 1) // 2)
    padded = with_halo(fields, (("gx", 2), ("gy", 3)), HW)
    padded = jnp.concatenate([padded[:, -HW:], padded, padded[:, :HW]], axis=1)
    own_tiles = dense_list[self_row, self_column]
    own_targets = filter_device[self_row, self_column]
    is_listed = own_targets >= 0
    before_mask = lax.broadcasted_iota(
        jnp.int32, (list_length, list_length), 0
    ) < lax.broadcasted_iota(jnp.int32, (list_length, list_length), 1)
    same_target = own_targets[:, None] == own_targets[None, :]
    send_rank = jnp.sum((same_target & before_mask).astype(jnp.int32), axis=0)
    send_slot = jnp.where(is_listed, own_targets * CAP + send_rank, groups_x * CAP)
    group_targets = filter_device[self_row]
    group_tiles = dense_list[self_row]
    arriving = (group_targets == self_column).astype(jnp.int32)
    row_rank = jnp.cumsum(arriving, axis=1) - arriving
    source_no = lax.broadcasted_iota(jnp.int32, (groups_x, list_length), 0)
    arrival_slot = (source_no * CAP + row_rank).reshape(-1)
    arrival_order = jnp.cumsum(arriving.reshape(-1)) - 1
    arrival_pos = jnp.where(arriving.reshape(-1) > 0, arrival_order, per_filter)
    take_slot = jnp.zeros((per_filter,), jnp.int32).at[arrival_pos].set(arrival_slot, mode="drop")
    take_tile = (
        jnp.zeros((per_filter,), jnp.int32)
        .at[arrival_pos]
        .set(group_tiles.reshape(-1), mode="drop")
    )
    take_source = (
        jnp.zeros((per_filter,), jnp.int32).at[arrival_pos].set(source_no.reshape(-1), mode="drop")
    )
    own_cut = cut_tiles(padded, jnp.where(is_listed, own_tiles, 0), across_x, across_y)
    own_statistics = tile_statistics(own_cut)
    stat_length = own_statistics.shape[1]
    outgoing = (
        jnp.zeros((groups_x * CAP, stat_length), jnp.float32)
        .at[send_slot]
        .set(own_statistics, mode="drop")
        .reshape(groups_x, CAP, stat_length)
    )
    incoming = lax.all_to_all(outgoing, "gx", split_axis=0, concat_axis=0, tiled=True)
    statistics = incoming.reshape(groups_x * CAP, stat_length)[take_slot]
    tile_means = jnp.mean(
        statistics.reshape(per_filter, HW * 8, stat_length // (HW * 8)), axis=2
    )
    tile_x = take_source * across_x + take_tile // across_y % across_x
    tile_y = self_row * across_y + take_tile % across_y
    pencils = pencil_order.shape[0]
    coarse_x = across_x * groups_x // 2
    per_row = pencils // groups_y
    local_pencil = tile_y // 2 - self_row * per_row
    cell_no = local_pencil * coarse_x + tile_x // 2
    placing = (
        lax.broadcasted_iota(jnp.int32, (per_row * coarse_x, per_filter), 0) == cell_no[None, :]
    ).astype(jnp.float32)
    partial_sums = jnp.dot(
        placing, tile_means, precision=HIGHEST, preferred_element_type=jnp.float32
    ).reshape(per_row, coarse_x * HW * 8)
    row_sums = lax.psum(partial_sums, "gx")
    all_rows = lax.all_gather(row_sums, "gy", axis=0, tiled=True)
    row_pencils = lax.dynamic_slice_in_dim(pencil_order, self_row * per_row, per_row)
    own_rows = all_rows[row_pencils]
    every_tile = dense_list.reshape(-1)
    every_valid = every_tile >= 0
    every_group = lax.broadcasted_iota(jnp.int32, dense_list.shape, 0).reshape(-1)
    every_source = lax.broadcasted_iota(jnp.int32, dense_list.shape, 1).reshape(-1)
    every_y = (every_group * across_y + every_tile % across_y) // 2
    every_x = (every_source * across_x + every_tile // across_y % across_x) // 2
    in_row = ((row_pencils[:, None] == every_y[None, :]) & every_valid[None, :]).astype(jnp.float32)
    in_column = (
        every_x[:, None] == lax.broadcasted_iota(jnp.int32, (every_x.shape[0], coarse_x), 1)
    ).astype(jnp.float32)
    tile_counts = jnp.dot(in_row, in_column, precision=HIGHEST, preferred_element_type=jnp.float32)
    averaged = (
        own_rows.reshape(per_row, coarse_x, HW * 8) / jnp.maximum(tile_counts, 1.0)[:, :, None]
    )
    return (statistics, averaged.reshape(per_row, coarse_x * HW * 8))


def solution(mesh):
    in_specs = (P(None, None, "gx", "gy"), P(), P(), P())
    out_specs = (P(("gx", "gy"), None), P("gy", None))
    return jax.shard_map(shards, mesh=mesh, in_specs=in_specs, out_specs=out_specs, check_vma=False)
```

```python
import jax
import jax.numpy as jnp
from jax import lax
from jax.sharding import PartitionSpec as P

TE = 16
HW = 4
CAP = 2


HIGHEST = lax.Precision.HIGHEST


def with_halo(block, sides, width):
    for axis, dim in sides:
        count = lax.axis_size(axis)
        forward = [(i, i + 1) for i in range(count - 1)]
        forward.append((count - 1, 0))
        backward = [(target, source) for source, target in forward]
        low = lax.ppermute(
            lax.slice_in_dim(block, block.shape[dim] - width, None, axis=dim), axis, forward
        )
        high = lax.ppermute(lax.slice_in_dim(block, 0, width, axis=dim), axis, backward)
        block = jnp.concatenate([low, block, high], axis=dim)
    return block


def band_matrix(half_width):
    span = TE + 2 * HW
    row_index = lax.broadcasted_iota(jnp.int32, (TE, span), 0)
    column_index = lax.broadcasted_iota(jnp.int32, (TE, span), 1)
    inside = jnp.abs(column_index - row_index - HW) <= half_width
    return jnp.where(inside, 1.0 / (2 * half_width + 1), 0.0).astype(jnp.float32)


def plane_matrix(half_width):
    span = TE + 2 * HW
    weights = band_matrix(half_width)
    return jnp.einsum("ax,by->xyab", weights, weights, precision=HIGHEST).reshape(
        span * span, TE * TE
    )


def box_band(columns, half_width):
    along_z = jnp.einsum("az,qtzp->qtap", band_matrix(half_width), columns, precision=HIGHEST)
    return jnp.einsum("qtap,pc->qtac", along_z, plane_matrix(half_width), precision=HIGHEST)


def quantities(tiles):
    span = TE + 2 * HW
    tile_count = tiles.shape[0]
    cell_values = tiles.astype(jnp.float32).reshape(tile_count, tiles.shape[1], span, span * span)
    solid = cell_values[:, 0]
    gas_speed = [cell_values[:, 1 + direction] for direction in range(3)]
    grain_speed = [cell_values[:, 4 + direction] for direction in range(3)]
    pressure = cell_values[:, 7]
    granular = cell_values[:, 8]
    friction = cell_values[:, 9]
    quantity_list = [solid] + gas_speed + [pressure, friction]
    quantity_list = quantity_list + [solid * speed for speed in gas_speed]
    quantity_list = quantity_list + [solid * speed for speed in grain_speed]
    quantity_list = quantity_list + [solid * granular, solid * pressure]
    quantity_list = quantity_list + [
        friction * (gas_speed[direction] - grain_speed[direction]) for direction in range(3)
    ]
    return jnp.stack(quantity_list, axis=0)


def block_matrix():
    sub_edge = TE // 4
    plane_index = lax.broadcasted_iota(jnp.int32, (TE * TE, sub_edge * sub_edge), 0)
    block_index = lax.broadcasted_iota(jnp.int32, (TE * TE, sub_edge * sub_edge), 1)
    block_of = plane_index // TE // 4 * sub_edge + plane_index % TE // 4
    return jnp.where(block_of == block_index, 1.0 / 16.0, 0.0).astype(jnp.float32)


def closure_blocks(smoothed):
    solid_mean = smoothed[0]
    components = []
    for direction in range(3):
        components.append(smoothed[6 + direction] / solid_mean - smoothed[1 + direction])
    for direction in range(3):
        components.append(
            smoothed[14 + direction]
            - smoothed[5] * (smoothed[6 + direction] - smoothed[9 + direction]) / solid_mean
        )
    components.append(smoothed[12] / solid_mean)
    components.append(smoothed[13] / solid_mean - smoothed[4])
    sub_edge = TE // 4
    stacked = jnp.stack(components, axis=0)
    tile_count = stacked.shape[1]
    depth_mean = jnp.mean(stacked.reshape(8, tile_count, sub_edge, 4, TE * TE), axis=3)
    blocks = jnp.einsum("ktzp,pc->ktzc", depth_mean, block_matrix(), precision=HIGHEST)
    return blocks.reshape(8, tile_count, sub_edge**3)


def plane_ones(half_width):
    span = TE + 2 * HW
    row_index = lax.broadcasted_iota(jnp.int32, (TE, span), 0)
    column_index = lax.broadcasted_iota(jnp.int32, (TE, span), 1)
    inside = (jnp.abs(column_index - row_index - HW) <= half_width).astype(jnp.float32)
    return (
        jnp.einsum("ax,by->xyab", inside, inside, precision=HIGHEST)
        .reshape(span * span, TE * TE)
        .astype(jnp.bfloat16)
    )


def split_three(values):
    high = lax.reduce_precision(values, exponent_bits=8, mantissa_bits=7)
    rest = values - high
    middle = lax.reduce_precision(rest, exponent_bits=8, mantissa_bits=7)
    low = rest - middle
    return jnp.stack([high, middle, low], axis=0).astype(jnp.bfloat16)


def tile_statistics(tiles):
    total_tiles = tiles.shape[0]
    columns = quantities(tiles)
    results = []
    for half_width in range(1, HW + 1):
        window = 2 * half_width + 1
        depth_sum = columns[:, :, HW - half_width : HW - half_width + TE]
        for step in range(1, window):
            start = HW - half_width + step
            depth_sum = depth_sum + columns[:, :, start : start + TE]
        pieces = split_three(depth_sum)
        plane = jnp.dot(pieces, plane_ones(half_width), preferred_element_type=jnp.float32)
        smoothed = (plane[0] + plane[1] + plane[2]) / float(window**3)
        results.append(closure_blocks(smoothed))
    mapped = jnp.stack(results, axis=0)
    return jnp.transpose(mapped, (2, 0, 1, 3)).reshape(total_tiles, HW * 8 * (TE // 4) ** 3)


def cut_tiles(padded, tile_ids, across_x, across_y):
    span = TE + 2 * HW
    depth_at = tile_ids // (across_x * across_y)
    column_at = tile_ids // across_y % across_x
    row_at = tile_ids % across_y

    def single_tile(depth_one, column_one, row_one):
        return lax.dynamic_slice(
            padded,
            (jnp.int32(0), depth_one * TE, column_one * TE, row_one * TE),
            (padded.shape[0], span, span, span),
        )

    pieces = jax.vmap(single_tile)(depth_at, column_at, row_at)
    return pieces.reshape(tile_ids.shape[0], padded.shape[0], span * span * span)


def shards(fields, dense_list, filter_device, pencil_order):
    groups_x = lax.axis_size("gx")
    groups_y = lax.axis_size("gy")
    self_column = lax.axis_index("gx")
    self_row = lax.axis_index("gy")
    across_x = fields.shape[2] // TE
    across_y = fields.shape[3] // TE
    list_length = dense_list.shape[2]
    per_filter = groups_x // 4 * (CAP + (CAP - 1) // 2)
    padded = with_halo(fields, (("gx", 2), ("gy", 3)), HW)
    padded = jnp.concatenate([padded[:, -HW:], padded, padded[:, :HW]], axis=1)
    own_tiles = dense_list[self_row, self_column]
    own_targets = filter_device[self_row, self_column]
    is_listed = own_targets >= 0
    before_mask = lax.broadcasted_iota(
        jnp.int32, (list_length, list_length), 0
    ) < lax.broadcasted_iota(jnp.int32, (list_length, list_length), 1)
    same_target = own_targets[:, None] == own_targets[None, :]
    send_rank = jnp.sum((same_target & before_mask).astype(jnp.int32), axis=0)
    send_slot = jnp.where(is_listed, own_targets * CAP + send_rank, groups_x * CAP)
    group_targets = filter_device[self_row]
    group_tiles = dense_list[self_row]
    arriving = (group_targets == self_column).astype(jnp.int32)
    row_rank = jnp.cumsum(arriving, axis=1) - arriving
    source_no = lax.broadcasted_iota(jnp.int32, (groups_x, list_length), 0)
    arrival_slot = (source_no * CAP + row_rank).reshape(-1)
    arrival_order = jnp.cumsum(arriving.reshape(-1)) - 1
    arrival_pos = jnp.where(arriving.reshape(-1) > 0, arrival_order, per_filter)
    take_slot = jnp.zeros((per_filter,), jnp.int32).at[arrival_pos].set(arrival_slot, mode="drop")
    take_tile = (
        jnp.zeros((per_filter,), jnp.int32)
        .at[arrival_pos]
        .set(group_tiles.reshape(-1), mode="drop")
    )
    take_source = (
        jnp.zeros((per_filter,), jnp.int32).at[arrival_pos].set(source_no.reshape(-1), mode="drop")
    )
    own_cut = cut_tiles(padded, jnp.where(is_listed, own_tiles, 0), across_x, across_y)
    own_statistics = tile_statistics(own_cut)
    stat_length = own_statistics.shape[1]
    outgoing = (
        jnp.zeros((groups_x * CAP, stat_length), jnp.float32)
        .at[send_slot]
        .set(own_statistics, mode="drop")
        .reshape(groups_x, CAP, stat_length)
    )
    incoming = lax.all_to_all(outgoing, "gx", split_axis=0, concat_axis=0, tiled=True)
    statistics = incoming.reshape(groups_x * CAP, stat_length)[take_slot]
    own_means = jnp.where(
        is_listed[:, None],
        jnp.mean(own_statistics.reshape(list_length, HW * 8, stat_length // (HW * 8)), axis=2),
        0.0,
    )
    every_means = lax.all_gather(own_means, ("gx", "gy"), axis=0, tiled=False)
    every_means = jnp.transpose(
        every_means.reshape(groups_x, groups_y, list_length, HW * 8), (1, 0, 2, 3)
    ).reshape(groups_y * groups_x * list_length, HW * 8)
    pencils = pencil_order.shape[0]
    coarse_x = across_x * groups_x // 2
    per_row = pencils // groups_y
    row_pencils = lax.dynamic_slice_in_dim(pencil_order, self_row * per_row, per_row)
    every_tile = dense_list.reshape(-1)
    every_valid = every_tile >= 0
    every_group = lax.broadcasted_iota(jnp.int32, dense_list.shape, 0).reshape(-1)
    every_source = lax.broadcasted_iota(jnp.int32, dense_list.shape, 1).reshape(-1)
    every_y = (every_group * across_y + every_tile % across_y) // 2
    every_x = (every_source * across_x + every_tile // across_y % across_x) // 2
    in_row = ((row_pencils[:, None] == every_y[None, :]) & every_valid[None, :]).astype(jnp.float32)
    in_column = (
        every_x[:, None] == lax.broadcasted_iota(jnp.int32, (every_x.shape[0], coarse_x), 1)
    ).astype(jnp.float32)
    tile_counts = jnp.dot(in_row, in_column, precision=HIGHEST, preferred_element_type=jnp.float32)
    cell_sums = jnp.einsum(
        "rj,jc,jk->rck", in_row, in_column, every_means, precision=HIGHEST
    )
    averaged = cell_sums / jnp.maximum(tile_counts, 1.0)[:, :, None]
    return (statistics, averaged.reshape(per_row, coarse_x * HW * 8))


def solution(mesh):
    in_specs = (P(None, None, "gx", "gy"), P(), P(), P())
    out_specs = (P(("gx", "gy"), None), P("gy", None))
    return jax.shard_map(shards, mesh=mesh, in_specs=in_specs, out_specs=out_specs, check_vma=False)
```

```python
import jax
import jax.numpy as jnp
from jax import lax
from jax.sharding import PartitionSpec as P

TE = 16
HW = 4
CAP = 2


HIGHEST = lax.Precision.HIGHEST


def with_halo(block, sides, width):
    for axis, dim in sides:
        count = lax.axis_size(axis)
        forward = [(i, i + 1) for i in range(count - 1)]
        forward.append((count - 1, 0))
        backward = [(target, source) for source, target in forward]
        low = lax.ppermute(
            lax.slice_in_dim(block, block.shape[dim] - width, None, axis=dim), axis, forward
        )
        high = lax.ppermute(lax.slice_in_dim(block, 0, width, axis=dim), axis, backward)
        block = jnp.concatenate([low, block, high], axis=dim)
    return block


def band_matrix(half_width):
    span = TE + 2 * HW
    row_index = lax.broadcasted_iota(jnp.int32, (TE, span), 0)
    column_index = lax.broadcasted_iota(jnp.int32, (TE, span), 1)
    inside = jnp.abs(column_index - row_index - HW) <= half_width
    return jnp.where(inside, 1.0 / (2 * half_width + 1), 0.0).astype(jnp.float32)


def plane_matrix(half_width):
    span = TE + 2 * HW
    weights = band_matrix(half_width)
    return jnp.einsum("ax,by->xyab", weights, weights, precision=HIGHEST).reshape(
        span * span, TE * TE
    )


def box_band(columns, half_width):
    along_z = jnp.einsum("az,qtzp->qtap", band_matrix(half_width), columns, precision=HIGHEST)
    return jnp.einsum("qtap,pc->qtac", along_z, plane_matrix(half_width), precision=HIGHEST)


def quantities(tiles):
    span = TE + 2 * HW
    tile_count = tiles.shape[0]
    cell_values = tiles.astype(jnp.float32).reshape(tile_count, tiles.shape[1], span, span * span)
    solid = cell_values[:, 0]
    gas_speed = [cell_values[:, 1 + direction] for direction in range(3)]
    grain_speed = [cell_values[:, 4 + direction] for direction in range(3)]
    pressure = cell_values[:, 7]
    granular = cell_values[:, 8]
    friction = cell_values[:, 9]
    quantity_list = [solid] + gas_speed + [pressure, friction]
    quantity_list = quantity_list + [solid * speed for speed in gas_speed]
    quantity_list = quantity_list + [solid * speed for speed in grain_speed]
    quantity_list = quantity_list + [solid * granular, solid * pressure]
    quantity_list = quantity_list + [
        friction * (gas_speed[direction] - grain_speed[direction]) for direction in range(3)
    ]
    return jnp.stack(quantity_list, axis=0)


def block_matrix():
    sub_edge = TE // 4
    plane_index = lax.broadcasted_iota(jnp.int32, (TE * TE, sub_edge * sub_edge), 0)
    block_index = lax.broadcasted_iota(jnp.int32, (TE * TE, sub_edge * sub_edge), 1)
    block_of = plane_index // TE // 4 * sub_edge + plane_index % TE // 4
    return jnp.where(block_of == block_index, 1.0 / 16.0, 0.0).astype(jnp.float32)


def closure_blocks(smoothed):
    solid_mean = smoothed[0]
    components = []
    for direction in range(3):
        components.append(smoothed[6 + direction] / solid_mean - smoothed[1 + direction])
    for direction in range(3):
        components.append(
            smoothed[14 + direction]
            - smoothed[5] * (smoothed[6 + direction] - smoothed[9 + direction]) / solid_mean
        )
    components.append(smoothed[12] / solid_mean)
    components.append(smoothed[13] / solid_mean - smoothed[4])
    sub_edge = TE // 4
    stacked = jnp.stack(components, axis=0)
    tile_count = stacked.shape[1]
    depth_mean = jnp.mean(stacked.reshape(8, tile_count, sub_edge, 4, TE * TE), axis=3)
    blocks = jnp.einsum("ktzp,pc->ktzc", depth_mean, block_matrix(), precision=HIGHEST)
    return blocks.reshape(8, tile_count, sub_edge**3)


def tile_statistics(tiles):
    total_tiles = tiles.shape[0]
    columns = quantities(tiles)
    results = []
    for half_width in range(1, HW + 1):
        results.append(closure_blocks(box_band(columns, half_width)))
    mapped = jnp.stack(results, axis=0)
    return jnp.transpose(mapped, (2, 0, 1, 3)).reshape(total_tiles, HW * 8 * (TE // 4) ** 3)


def cut_tiles(padded, tile_ids, across_x, across_y):
    span = TE + 2 * HW
    depth_at = tile_ids // (across_x * across_y)
    column_at = tile_ids // across_y % across_x
    row_at = tile_ids % across_y

    def single_tile(depth_one, column_one, row_one):
        return lax.dynamic_slice(
            padded,
            (jnp.int32(0), depth_one * TE, column_one * TE, row_one * TE),
            (padded.shape[0], span, span, span),
        )

    pieces = jax.vmap(single_tile)(depth_at, column_at, row_at)
    return pieces.reshape(tile_ids.shape[0], padded.shape[0], span * span * span)


def shards(fields, dense_list, filter_device, pencil_order):
    groups_x = lax.axis_size("gx")
    groups_y = lax.axis_size("gy")
    self_column = lax.axis_index("gx")
    self_row = lax.axis_index("gy")
    across_x = fields.shape[2] // TE
    across_y = fields.shape[3] // TE
    list_length = dense_list.shape[2]
    per_filter = groups_x // 4 * (CAP + (CAP - 1) // 2)
    padded = with_halo(fields, (("gx", 2), ("gy", 3)), HW)
    padded = jnp.concatenate([padded[:, -HW:], padded, padded[:, :HW]], axis=1)
    own_tiles = dense_list[self_row, self_column]
    own_targets = filter_device[self_row, self_column]
    is_listed = own_targets >= 0
    before_mask = lax.broadcasted_iota(
        jnp.int32, (list_length, list_length), 0
    ) < lax.broadcasted_iota(jnp.int32, (list_length, list_length), 1)
    same_target = own_targets[:, None] == own_targets[None, :]
    send_rank = jnp.sum((same_target & before_mask).astype(jnp.int32), axis=0)
    send_slot = jnp.where(is_listed, own_targets * CAP + send_rank, groups_x * CAP)
    group_targets = filter_device[self_row]
    group_tiles = dense_list[self_row]
    arriving = (group_targets == self_column).astype(jnp.int32)
    row_rank = jnp.cumsum(arriving, axis=1) - arriving
    source_no = lax.broadcasted_iota(jnp.int32, (groups_x, list_length), 0)
    arrival_slot = (source_no * CAP + row_rank).reshape(-1)
    arrival_order = jnp.cumsum(arriving.reshape(-1)) - 1
    arrival_pos = jnp.where(arriving.reshape(-1) > 0, arrival_order, per_filter)
    take_slot = jnp.zeros((per_filter,), jnp.int32).at[arrival_pos].set(arrival_slot, mode="drop")
    take_tile = (
        jnp.zeros((per_filter,), jnp.int32)
        .at[arrival_pos]
        .set(group_tiles.reshape(-1), mode="drop")
    )
    take_source = (
        jnp.zeros((per_filter,), jnp.int32).at[arrival_pos].set(source_no.reshape(-1), mode="drop")
    )
    own_cut = cut_tiles(padded, jnp.where(is_listed, own_tiles, 0), across_x, across_y)
    own_statistics = tile_statistics(own_cut)
    stat_length = own_statistics.shape[1]
    outgoing = (
        jnp.zeros((groups_x * CAP, stat_length), jnp.float32)
        .at[send_slot]
        .set(own_statistics, mode="drop")
        .reshape(groups_x, CAP, stat_length)
    )
    incoming = lax.all_to_all(outgoing, "gx", split_axis=0, concat_axis=0, tiled=True)
    statistics = incoming.reshape(groups_x * CAP, stat_length)[take_slot]
    own_means = jnp.where(
        is_listed[:, None],
        jnp.mean(own_statistics.reshape(list_length, HW * 8, stat_length // (HW * 8)), axis=2),
        0.0,
    )
    every_means = lax.all_gather(own_means, ("gx", "gy"), axis=0, tiled=False)
    every_means = jnp.transpose(
        every_means.reshape(groups_x, groups_y, list_length, HW * 8), (1, 0, 2, 3)
    ).reshape(groups_y * groups_x * list_length, HW * 8)
    pencils = pencil_order.shape[0]
    coarse_x = across_x * groups_x // 2
    per_row = pencils // groups_y
    row_pencils = lax.dynamic_slice_in_dim(pencil_order, self_row * per_row, per_row)
    every_tile = dense_list.reshape(-1)
    every_valid = every_tile >= 0
    every_group = lax.broadcasted_iota(jnp.int32, dense_list.shape, 0).reshape(-1)
    every_source = lax.broadcasted_iota(jnp.int32, dense_list.shape, 1).reshape(-1)
    every_y = (every_group * across_y + every_tile % across_y) // 2
    every_x = (every_source * across_x + every_tile // across_y % across_x) // 2
    in_row = ((row_pencils[:, None] == every_y[None, :]) & every_valid[None, :]).astype(jnp.float32)
    in_column = (
        every_x[:, None] == lax.broadcasted_iota(jnp.int32, (every_x.shape[0], coarse_x), 1)
    ).astype(jnp.float32)
    tile_counts = jnp.dot(in_row, in_column, precision=HIGHEST, preferred_element_type=jnp.float32)
    cell_sums = jnp.einsum(
        "rj,jc,jk->rck", in_row, in_column, every_means, precision=HIGHEST
    )
    averaged = cell_sums / jnp.maximum(tile_counts, 1.0)[:, :, None]
    return (statistics, averaged.reshape(per_row, coarse_x * HW * 8))


def solution(mesh):
    in_specs = (P(None, None, "gx", "gy"), P(), P(), P())
    out_specs = (P(("gx", "gy"), None), P("gy", None))
    return jax.shard_map(shards, mesh=mesh, in_specs=in_specs, out_specs=out_specs, check_vma=False)
```

```python
import jax
import jax.numpy as jnp
from jax import lax
from jax.sharding import PartitionSpec as P

TE = 16
HW = 4
CAP = 2


HIGHEST = lax.Precision.HIGHEST


def with_halo(block, sides, width):
    for axis, dim in sides:
        count = lax.axis_size(axis)
        forward = [(i, i + 1) for i in range(count - 1)]
        forward.append((count - 1, 0))
        backward = [(target, source) for source, target in forward]
        low = lax.ppermute(
            lax.slice_in_dim(block, block.shape[dim] - width, None, axis=dim), axis, forward
        )
        high = lax.ppermute(lax.slice_in_dim(block, 0, width, axis=dim), axis, backward)
        block = jnp.concatenate([low, block, high], axis=dim)
    return block


def band_matrix(half_width):
    span = TE + 2 * HW
    row_index = lax.broadcasted_iota(jnp.int32, (TE, span), 0)
    column_index = lax.broadcasted_iota(jnp.int32, (TE, span), 1)
    inside = jnp.abs(column_index - row_index - HW) <= half_width
    return jnp.where(inside, 1.0 / (2 * half_width + 1), 0.0).astype(jnp.float32)


def plane_matrix(half_width):
    span = TE + 2 * HW
    weights = band_matrix(half_width)
    return jnp.einsum("ax,by->xyab", weights, weights, precision=HIGHEST).reshape(
        span * span, TE * TE
    )


def box_band(columns, half_width):
    along_z = jnp.einsum("az,qtzp->qtap", band_matrix(half_width), columns, precision=HIGHEST)
    return jnp.einsum("qtap,pc->qtac", along_z, plane_matrix(half_width), precision=HIGHEST)


def quantities(tiles):
    span = TE + 2 * HW
    tile_count = tiles.shape[0]
    cell_values = tiles.astype(jnp.float32).reshape(tile_count, tiles.shape[1], span, span * span)
    solid = cell_values[:, 0]
    gas_speed = [cell_values[:, 1 + direction] for direction in range(3)]
    grain_speed = [cell_values[:, 4 + direction] for direction in range(3)]
    pressure = cell_values[:, 7]
    granular = cell_values[:, 8]
    friction = cell_values[:, 9]
    quantity_list = [solid] + gas_speed + [pressure, friction]
    quantity_list = quantity_list + [solid * speed for speed in gas_speed]
    quantity_list = quantity_list + [solid * speed for speed in grain_speed]
    quantity_list = quantity_list + [solid * granular, solid * pressure]
    quantity_list = quantity_list + [
        friction * (gas_speed[direction] - grain_speed[direction]) for direction in range(3)
    ]
    return jnp.stack(quantity_list, axis=0)


def block_matrix():
    sub_edge = TE // 4
    plane_index = lax.broadcasted_iota(jnp.int32, (TE * TE, sub_edge * sub_edge), 0)
    block_index = lax.broadcasted_iota(jnp.int32, (TE * TE, sub_edge * sub_edge), 1)
    block_of = plane_index // TE // 4 * sub_edge + plane_index % TE // 4
    return jnp.where(block_of == block_index, 1.0 / 16.0, 0.0).astype(jnp.float32)


def closure_blocks(smoothed):
    solid_mean = smoothed[0]
    components = []
    for direction in range(3):
        components.append(smoothed[6 + direction] / solid_mean - smoothed[1 + direction])
    for direction in range(3):
        components.append(
            smoothed[14 + direction]
            - smoothed[5] * (smoothed[6 + direction] - smoothed[9 + direction]) / solid_mean
        )
    components.append(smoothed[12] / solid_mean)
    components.append(smoothed[13] / solid_mean - smoothed[4])
    sub_edge = TE // 4
    stacked = jnp.stack(components, axis=0)
    tile_count = stacked.shape[1]
    depth_mean = jnp.mean(stacked.reshape(8, tile_count, sub_edge, 4, TE * TE), axis=3)
    blocks = jnp.einsum("ktzp,pc->ktzc", depth_mean, block_matrix(), precision=HIGHEST)
    return blocks.reshape(8, tile_count, sub_edge**3)


def tile_statistics(tiles):
    total_tiles = tiles.shape[0]
    columns = quantities(tiles)
    results = []
    for half_width in range(1, HW + 1):
        results.append(closure_blocks(box_band(columns, half_width)))
    mapped = jnp.stack(results, axis=0)
    return jnp.transpose(mapped, (2, 0, 1, 3)).reshape(total_tiles, HW * 8 * (TE // 4) ** 3)


def cut_tiles(padded, tile_ids, across_x, across_y):
    span = TE + 2 * HW
    depth_at = tile_ids // (across_x * across_y)
    column_at = tile_ids // across_y % across_x
    row_at = tile_ids % across_y
    pieces = []
    for index in range(tile_ids.shape[0]):
        window = lax.dynamic_slice(
            padded,
            (jnp.int32(0), depth_at[index] * TE, column_at[index] * TE, row_at[index] * TE),
            (padded.shape[0], span, span, span),
        )
        pieces.append(window.reshape(padded.shape[0], span * span * span))
    return jnp.stack(pieces, axis=0)


def shards(fields, dense_list, filter_device, pencil_order):
    groups_x = lax.axis_size("gx")
    groups_y = lax.axis_size("gy")
    self_column = lax.axis_index("gx")
    self_row = lax.axis_index("gy")
    across_x = fields.shape[2] // TE
    across_y = fields.shape[3] // TE
    list_length = dense_list.shape[2]
    per_filter = groups_x // 4 * (CAP + (CAP - 1) // 2)
    padded = with_halo(fields, (("gx", 2), ("gy", 3)), HW)
    padded = jnp.concatenate([padded[:, -HW:], padded, padded[:, :HW]], axis=1)
    own_tiles = dense_list[self_row, self_column]
    own_targets = filter_device[self_row, self_column]
    is_listed = own_targets >= 0
    before_mask = lax.broadcasted_iota(
        jnp.int32, (list_length, list_length), 0
    ) < lax.broadcasted_iota(jnp.int32, (list_length, list_length), 1)
    same_target = own_targets[:, None] == own_targets[None, :]
    send_rank = jnp.sum((same_target & before_mask).astype(jnp.int32), axis=0)
    send_slot = jnp.where(is_listed, own_targets * CAP + send_rank, groups_x * CAP)
    group_targets = filter_device[self_row]
    group_tiles = dense_list[self_row]
    arriving = (group_targets == self_column).astype(jnp.int32)
    row_rank = jnp.cumsum(arriving, axis=1) - arriving
    source_no = lax.broadcasted_iota(jnp.int32, (groups_x, list_length), 0)
    arrival_slot = (source_no * CAP + row_rank).reshape(-1)
    arrival_order = jnp.cumsum(arriving.reshape(-1)) - 1
    arrival_pos = jnp.where(arriving.reshape(-1) > 0, arrival_order, per_filter)
    take_slot = jnp.zeros((per_filter,), jnp.int32).at[arrival_pos].set(arrival_slot, mode="drop")
    take_tile = (
        jnp.zeros((per_filter,), jnp.int32)
        .at[arrival_pos]
        .set(group_tiles.reshape(-1), mode="drop")
    )
    take_source = (
        jnp.zeros((per_filter,), jnp.int32).at[arrival_pos].set(source_no.reshape(-1), mode="drop")
    )
    own_cut = cut_tiles(padded, jnp.where(is_listed, own_tiles, 0), across_x, across_y)
    own_statistics = tile_statistics(own_cut)
    stat_length = own_statistics.shape[1]
    outgoing = (
        jnp.zeros((groups_x * CAP, stat_length), jnp.float32)
        .at[send_slot]
        .set(own_statistics, mode="drop")
        .reshape(groups_x, CAP, stat_length)
    )
    incoming = lax.all_to_all(outgoing, "gx", split_axis=0, concat_axis=0, tiled=True)
    statistics = incoming.reshape(groups_x * CAP, stat_length)[take_slot]
    own_means = jnp.where(
        is_listed[:, None],
        jnp.mean(own_statistics.reshape(list_length, HW * 8, stat_length // (HW * 8)), axis=2),
        0.0,
    )
    every_means = lax.all_gather(own_means, ("gx", "gy"), axis=0, tiled=False)
    every_means = jnp.transpose(
        every_means.reshape(groups_x, groups_y, list_length, HW * 8), (1, 0, 2, 3)
    ).reshape(groups_y * groups_x * list_length, HW * 8)
    pencils = pencil_order.shape[0]
    coarse_x = across_x * groups_x // 2
    per_row = pencils // groups_y
    row_pencils = lax.dynamic_slice_in_dim(pencil_order, self_row * per_row, per_row)
    every_tile = dense_list.reshape(-1)
    every_valid = every_tile >= 0
    every_group = lax.broadcasted_iota(jnp.int32, dense_list.shape, 0).reshape(-1)
    every_source = lax.broadcasted_iota(jnp.int32, dense_list.shape, 1).reshape(-1)
    every_y = (every_group * across_y + every_tile % across_y) // 2
    every_x = (every_source * across_x + every_tile // across_y % across_x) // 2
    in_row = ((row_pencils[:, None] == every_y[None, :]) & every_valid[None, :]).astype(jnp.float32)
    in_column = (
        every_x[:, None] == lax.broadcasted_iota(jnp.int32, (every_x.shape[0], coarse_x), 1)
    ).astype(jnp.float32)
    tile_counts = jnp.dot(in_row, in_column, precision=HIGHEST, preferred_element_type=jnp.float32)
    cell_sums = jnp.einsum(
        "rj,jc,jk->rck", in_row, in_column, every_means, precision=HIGHEST
    )
    averaged = cell_sums / jnp.maximum(tile_counts, 1.0)[:, :, None]
    return (statistics, averaged.reshape(per_row, coarse_x * HW * 8))


def solution(mesh):
    in_specs = (P(None, None, "gx", "gy"), P(), P(), P())
    out_specs = (P(("gx", "gy"), None), P("gy", None))
    return jax.shard_map(shards, mesh=mesh, in_specs=in_specs, out_specs=out_specs, check_vma=False)
```

```python
import numpy as np
import jax
import jax.numpy as jnp
from jax import lax
from jax.sharding import PartitionSpec as P

TE = 16
HW = 4
CAP = 2


HIGHEST = lax.Precision.HIGHEST


def with_halo(block, sides, width):
    for axis, dim in sides:
        count = lax.axis_size(axis)
        forward = [(i, i + 1) for i in range(count - 1)]
        forward.append((count - 1, 0))
        backward = [(target, source) for source, target in forward]
        low = lax.ppermute(
            lax.slice_in_dim(block, block.shape[dim] - width, None, axis=dim), axis, forward
        )
        high = lax.ppermute(lax.slice_in_dim(block, 0, width, axis=dim), axis, backward)
        block = jnp.concatenate([low, block, high], axis=dim)
    return block


def band_matrix(half_width):
    span = TE + 2 * HW
    row_index = np.arange(TE)[:, None]
    column_index = np.arange(span)[None, :]
    inside = np.abs(column_index - row_index - HW) <= half_width
    return np.where(inside, np.float32(1.0 / (2 * half_width + 1)), np.float32(0.0)).astype(np.float32)


def plane_matrix(half_width):
    span = TE + 2 * HW
    weights = band_matrix(half_width).astype(np.float64)
    return np.einsum("ax,by->xyab", weights, weights).reshape(span * span, TE * TE).astype(np.float32)


def box_band(columns, half_width):
    along_z = jnp.einsum("az,qtzp->qtap", band_matrix(half_width), columns, precision=HIGHEST)
    return jnp.einsum("qtap,pc->qtac", along_z, plane_matrix(half_width), precision=HIGHEST)


def quantities(tiles):
    span = TE + 2 * HW
    tile_count = tiles.shape[0]
    cell_values = tiles.astype(jnp.float32).reshape(tile_count, tiles.shape[1], span, span * span)
    solid = cell_values[:, 0]
    gas_speed = [cell_values[:, 1 + direction] for direction in range(3)]
    grain_speed = [cell_values[:, 4 + direction] for direction in range(3)]
    pressure = cell_values[:, 7]
    granular = cell_values[:, 8]
    friction = cell_values[:, 9]
    quantity_list = [solid] + gas_speed + [pressure, friction]
    quantity_list = quantity_list + [solid * speed for speed in gas_speed]
    quantity_list = quantity_list + [solid * speed for speed in grain_speed]
    quantity_list = quantity_list + [solid * granular, solid * pressure]
    quantity_list = quantity_list + [
        friction * (gas_speed[direction] - grain_speed[direction]) for direction in range(3)
    ]
    return jnp.stack(quantity_list, axis=0)


def block_matrix():
    sub_edge = TE // 4
    plane_index = np.arange(TE * TE)[:, None]
    block_index = np.arange(sub_edge * sub_edge)[None, :]
    block_of = plane_index // TE // 4 * sub_edge + plane_index % TE // 4
    return np.where(block_of == block_index, np.float32(1.0 / 16.0), np.float32(0.0)).astype(np.float32)


def closure_blocks(smoothed):
    solid_mean = smoothed[0]
    components = []
    for direction in range(3):
        components.append(smoothed[6 + direction] / solid_mean - smoothed[1 + direction])
    for direction in range(3):
        components.append(
            smoothed[14 + direction]
            - smoothed[5] * (smoothed[6 + direction] - smoothed[9 + direction]) / solid_mean
        )
    components.append(smoothed[12] / solid_mean)
    components.append(smoothed[13] / solid_mean - smoothed[4])
    sub_edge = TE // 4
    tile_count = components[0].shape[0]
    depth_mean = jnp.stack(
        [
            jnp.mean(component.reshape(tile_count, sub_edge, 4, TE * TE), axis=2)
            for component in components
        ],
        axis=0,
    )
    blocks = jnp.einsum("ktzp,pc->ktzc", depth_mean, block_matrix(), precision=HIGHEST)
    return blocks.reshape(8, tile_count, sub_edge**3)


def tile_statistics(tiles):
    total_tiles = tiles.shape[0]
    columns = quantities(tiles)
    results = []
    for half_width in range(1, HW + 1):
        results.append(closure_blocks(box_band(columns, half_width)))
    mapped = jnp.stack(results, axis=0)
    return jnp.transpose(mapped, (2, 0, 1, 3)).reshape(total_tiles, HW * 8 * (TE // 4) ** 3)


def cut_tiles(padded, tile_ids, across_x, across_y):
    span = TE + 2 * HW
    depth_at = tile_ids // (across_x * across_y)
    column_at = tile_ids // across_y % across_x
    row_at = tile_ids % across_y
    pieces = []
    for index in range(tile_ids.shape[0]):
        window = lax.dynamic_slice(
            padded,
            (jnp.int32(0), depth_at[index] * TE, column_at[index] * TE, row_at[index] * TE),
            (padded.shape[0], span, span, span),
        )
        pieces.append(window.reshape(padded.shape[0], span * span * span))
    return jnp.stack(pieces, axis=0)


def shards(fields, dense_list, filter_device, pencil_order):
    groups_x = lax.axis_size("gx")
    groups_y = lax.axis_size("gy")
    self_column = lax.axis_index("gx")
    self_row = lax.axis_index("gy")
    across_x = fields.shape[2] // TE
    across_y = fields.shape[3] // TE
    list_length = dense_list.shape[2]
    per_filter = groups_x // 4 * (CAP + (CAP - 1) // 2)
    padded = with_halo(fields, (("gx", 2), ("gy", 3)), HW)
    padded = jnp.concatenate([padded[:, -HW:], padded, padded[:, :HW]], axis=1)
    own_tiles = dense_list[self_row, self_column]
    own_targets = filter_device[self_row, self_column]
    is_listed = own_targets >= 0
    before_mask = lax.broadcasted_iota(
        jnp.int32, (list_length, list_length), 0
    ) < lax.broadcasted_iota(jnp.int32, (list_length, list_length), 1)
    same_target = own_targets[:, None] == own_targets[None, :]
    send_rank = jnp.sum((same_target & before_mask).astype(jnp.int32), axis=0)
    send_slot = jnp.where(is_listed, own_targets * CAP + send_rank, groups_x * CAP)
    group_targets = filter_device[self_row]
    group_tiles = dense_list[self_row]
    arriving = (group_targets == self_column).astype(jnp.int32)
    row_rank = jnp.cumsum(arriving, axis=1) - arriving
    source_no = lax.broadcasted_iota(jnp.int32, (groups_x, list_length), 0)
    arrival_slot = (source_no * CAP + row_rank).reshape(-1)
    arrival_order = jnp.cumsum(arriving.reshape(-1)) - 1
    arrival_pos = jnp.where(arriving.reshape(-1) > 0, arrival_order, per_filter)
    take_slot = jnp.zeros((per_filter,), jnp.int32).at[arrival_pos].set(arrival_slot, mode="drop")
    take_tile = (
        jnp.zeros((per_filter,), jnp.int32)
        .at[arrival_pos]
        .set(group_tiles.reshape(-1), mode="drop")
    )
    take_source = (
        jnp.zeros((per_filter,), jnp.int32).at[arrival_pos].set(source_no.reshape(-1), mode="drop")
    )
    own_cut = cut_tiles(padded, jnp.where(is_listed, own_tiles, 0), across_x, across_y)
    own_statistics = tile_statistics(own_cut)
    stat_length = own_statistics.shape[1]
    outgoing = (
        jnp.zeros((groups_x * CAP, stat_length), jnp.float32)
        .at[send_slot]
        .set(own_statistics, mode="drop")
        .reshape(groups_x, CAP, stat_length)
    )
    incoming = lax.all_to_all(outgoing, "gx", split_axis=0, concat_axis=0, tiled=True)
    statistics = incoming.reshape(groups_x * CAP, stat_length)[take_slot]
    own_means = jnp.where(
        is_listed[:, None],
        jnp.mean(own_statistics.reshape(list_length, HW * 8, stat_length // (HW * 8)), axis=2),
        0.0,
    )
    every_means = lax.all_gather(own_means, ("gx", "gy"), axis=0, tiled=False)
    every_means = jnp.transpose(
        every_means.reshape(groups_x, groups_y, list_length, HW * 8), (1, 0, 2, 3)
    ).reshape(groups_y * groups_x * list_length, HW * 8)
    pencils = pencil_order.shape[0]
    coarse_x = across_x * groups_x // 2
    per_row = pencils // groups_y
    row_pencils = lax.dynamic_slice_in_dim(pencil_order, self_row * per_row, per_row)
    every_tile = dense_list.reshape(-1)
    every_valid = every_tile >= 0
    every_group = lax.broadcasted_iota(jnp.int32, dense_list.shape, 0).reshape(-1)
    every_source = lax.broadcasted_iota(jnp.int32, dense_list.shape, 1).reshape(-1)
    every_y = (every_group * across_y + every_tile % across_y) // 2
    every_x = (every_source * across_x + every_tile // across_y % across_x) // 2
    in_row = ((row_pencils[:, None] == every_y[None, :]) & every_valid[None, :]).astype(jnp.float32)
    in_column = (
        every_x[:, None] == lax.broadcasted_iota(jnp.int32, (every_x.shape[0], coarse_x), 1)
    ).astype(jnp.float32)
    tile_counts = jnp.dot(in_row, in_column, precision=HIGHEST, preferred_element_type=jnp.float32)
    cell_sums = jnp.einsum(
        "rj,jc,jk->rck", in_row, in_column, every_means, precision=HIGHEST
    )
    averaged = cell_sums / jnp.maximum(tile_counts, 1.0)[:, :, None]
    return (statistics, averaged.reshape(per_row, coarse_x * HW * 8))


def solution(mesh):
    in_specs = (P(None, None, "gx", "gy"), P(), P(), P())
    out_specs = (P(("gx", "gy"), None), P("gy", None))
    return jax.shard_map(shards, mesh=mesh, in_specs=in_specs, out_specs=out_specs, check_vma=False)
```

```python
import numpy as np
import jax
import jax.numpy as jnp
from jax import lax
from jax.sharding import PartitionSpec as P

TE = 16
HW = 4
CAP = 2


HIGHEST = lax.Precision.HIGHEST


def with_halo(block, sides, width):
    for axis, dim in sides:
        count = lax.axis_size(axis)
        forward = [(i, i + 1) for i in range(count - 1)]
        forward.append((count - 1, 0))
        backward = [(target, source) for source, target in forward]
        low = lax.ppermute(
            lax.slice_in_dim(block, block.shape[dim] - width, None, axis=dim), axis, forward
        )
        high = lax.ppermute(lax.slice_in_dim(block, 0, width, axis=dim), axis, backward)
        block = jnp.concatenate([low, block, high], axis=dim)
    return block


def band_matrix(half_width):
    span = TE + 2 * HW
    row_index = np.arange(TE)[:, None]
    column_index = np.arange(span)[None, :]
    inside = np.abs(column_index - row_index - HW) <= half_width
    return np.where(inside, np.float32(1.0 / (2 * half_width + 1)), np.float32(0.0)).astype(np.float32)


def plane_matrix(half_width):
    span = TE + 2 * HW
    weights = band_matrix(half_width).astype(np.float64)
    return np.einsum("ax,by->xyab", weights, weights).reshape(span * span, TE * TE).astype(np.float32)


def band_ones(half_width):
    span = TE + 2 * HW
    row_index = np.arange(TE)[:, None]
    column_index = np.arange(span)[None, :]
    return (np.abs(column_index - row_index - HW) <= half_width).astype(np.float32)


def box_band(columns, half_width):
    window = 2 * half_width + 1
    along_z = jnp.einsum(
        "az,qtzp->qtap", band_ones(half_width), columns, precision=lax.Precision.HIGH
    )
    weights = (plane_matrix(half_width).astype(np.float64) / window).astype(np.float32)
    return jnp.einsum("qtap,pc->qtac", along_z, weights, precision=HIGHEST)


def quantities(tiles):
    span = TE + 2 * HW
    tile_count = tiles.shape[0]
    cell_values = tiles.astype(jnp.float32).reshape(tile_count, tiles.shape[1], span, span * span)
    solid = cell_values[:, 0]
    gas_speed = [cell_values[:, 1 + direction] for direction in range(3)]
    grain_speed = [cell_values[:, 4 + direction] for direction in range(3)]
    pressure = cell_values[:, 7]
    granular = cell_values[:, 8]
    friction = cell_values[:, 9]
    quantity_list = [solid] + gas_speed + [pressure, friction]
    quantity_list = quantity_list + [solid * speed for speed in gas_speed]
    quantity_list = quantity_list + [solid * speed for speed in grain_speed]
    quantity_list = quantity_list + [solid * granular, solid * pressure]
    quantity_list = quantity_list + [
        friction * (gas_speed[direction] - grain_speed[direction]) for direction in range(3)
    ]
    return jnp.stack(quantity_list, axis=0)


def block_matrix():
    sub_edge = TE // 4
    plane_index = np.arange(TE * TE)[:, None]
    block_index = np.arange(sub_edge * sub_edge)[None, :]
    block_of = plane_index // TE // 4 * sub_edge + plane_index % TE // 4
    return np.where(block_of == block_index, np.float32(1.0 / 16.0), np.float32(0.0)).astype(np.float32)


def closure_blocks(smoothed):
    solid_mean = smoothed[0]
    components = []
    for direction in range(3):
        components.append(smoothed[6 + direction] / solid_mean - smoothed[1 + direction])
    for direction in range(3):
        components.append(
            smoothed[14 + direction]
            - smoothed[5] * (smoothed[6 + direction] - smoothed[9 + direction]) / solid_mean
        )
    components.append(smoothed[12] / solid_mean)
    components.append(smoothed[13] / solid_mean - smoothed[4])
    sub_edge = TE // 4
    tile_count = components[0].shape[0]
    depth_mean = jnp.stack(
        [
            jnp.mean(component.reshape(tile_count, sub_edge, 4, TE * TE), axis=2)
            for component in components
        ],
        axis=0,
    )
    blocks = jnp.einsum("ktzp,pc->ktzc", depth_mean, block_matrix(), precision=HIGHEST)
    return blocks.reshape(8, tile_count, sub_edge**3)


def tile_statistics(tiles):
    total_tiles = tiles.shape[0]
    columns = quantities(tiles)
    results = []
    for half_width in range(1, HW + 1):
        results.append(closure_blocks(box_band(columns, half_width)))
    mapped = jnp.stack(results, axis=0)
    return jnp.transpose(mapped, (2, 0, 1, 3)).reshape(total_tiles, HW * 8 * (TE // 4) ** 3)


def cut_tiles(padded, tile_ids, across_x, across_y):
    span = TE + 2 * HW
    depth_at = tile_ids // (across_x * across_y)
    column_at = tile_ids // across_y % across_x
    row_at = tile_ids % across_y
    pieces = []
    for index in range(tile_ids.shape[0]):
        window = lax.dynamic_slice(
            padded,
            (jnp.int32(0), depth_at[index] * TE, column_at[index] * TE, row_at[index] * TE),
            (padded.shape[0], span, span, span),
        )
        pieces.append(window.reshape(padded.shape[0], span * span * span))
    return jnp.stack(pieces, axis=0)


def shards(fields, dense_list, filter_device, pencil_order):
    groups_x = lax.axis_size("gx")
    groups_y = lax.axis_size("gy")
    self_column = lax.axis_index("gx")
    self_row = lax.axis_index("gy")
    across_x = fields.shape[2] // TE
    across_y = fields.shape[3] // TE
    list_length = dense_list.shape[2]
    per_filter = groups_x // 4 * (CAP + (CAP - 1) // 2)
    padded = with_halo(fields, (("gx", 2), ("gy", 3)), HW)
    padded = jnp.concatenate([padded[:, -HW:], padded, padded[:, :HW]], axis=1)
    own_tiles = dense_list[self_row, self_column]
    own_targets = filter_device[self_row, self_column]
    is_listed = own_targets >= 0
    before_mask = lax.broadcasted_iota(
        jnp.int32, (list_length, list_length), 0
    ) < lax.broadcasted_iota(jnp.int32, (list_length, list_length), 1)
    same_target = own_targets[:, None] == own_targets[None, :]
    send_rank = jnp.sum((same_target & before_mask).astype(jnp.int32), axis=0)
    send_slot = jnp.where(is_listed, own_targets * CAP + send_rank, groups_x * CAP)
    group_targets = filter_device[self_row]
    group_tiles = dense_list[self_row]
    arriving = (group_targets == self_column).astype(jnp.int32)
    row_rank = jnp.cumsum(arriving, axis=1) - arriving
    source_no = lax.broadcasted_iota(jnp.int32, (groups_x, list_length), 0)
    arrival_slot = (source_no * CAP + row_rank).reshape(-1)
    arrival_order = jnp.cumsum(arriving.reshape(-1)) - 1
    arrival_pos = jnp.where(arriving.reshape(-1) > 0, arrival_order, per_filter)
    take_slot = jnp.zeros((per_filter,), jnp.int32).at[arrival_pos].set(arrival_slot, mode="drop")
    take_tile = (
        jnp.zeros((per_filter,), jnp.int32)
        .at[arrival_pos]
        .set(group_tiles.reshape(-1), mode="drop")
    )
    take_source = (
        jnp.zeros((per_filter,), jnp.int32).at[arrival_pos].set(source_no.reshape(-1), mode="drop")
    )
    own_cut = cut_tiles(padded, jnp.where(is_listed, own_tiles, 0), across_x, across_y)
    own_statistics = tile_statistics(own_cut)
    stat_length = own_statistics.shape[1]
    outgoing = (
        jnp.zeros((groups_x * CAP, stat_length), jnp.float32)
        .at[send_slot]
        .set(own_statistics, mode="drop")
        .reshape(groups_x, CAP, stat_length)
    )
    incoming = lax.all_to_all(outgoing, "gx", split_axis=0, concat_axis=0, tiled=True)
    statistics = incoming.reshape(groups_x * CAP, stat_length)[take_slot]
    own_means = jnp.where(
        is_listed[:, None],
        jnp.mean(own_statistics.reshape(list_length, HW * 8, stat_length // (HW * 8)), axis=2),
        0.0,
    )
    every_means = lax.all_gather(own_means, ("gx", "gy"), axis=0, tiled=False)
    every_means = jnp.transpose(
        every_means.reshape(groups_x, groups_y, list_length, HW * 8), (1, 0, 2, 3)
    ).reshape(groups_y * groups_x * list_length, HW * 8)
    pencils = pencil_order.shape[0]
    coarse_x = across_x * groups_x // 2
    per_row = pencils // groups_y
    row_pencils = lax.dynamic_slice_in_dim(pencil_order, self_row * per_row, per_row)
    every_tile = dense_list.reshape(-1)
    every_valid = every_tile >= 0
    every_group = lax.broadcasted_iota(jnp.int32, dense_list.shape, 0).reshape(-1)
    every_source = lax.broadcasted_iota(jnp.int32, dense_list.shape, 1).reshape(-1)
    every_y = (every_group * across_y + every_tile % across_y) // 2
    every_x = (every_source * across_x + every_tile // across_y % across_x) // 2
    in_row = ((row_pencils[:, None] == every_y[None, :]) & every_valid[None, :]).astype(jnp.float32)
    in_column = (
        every_x[:, None] == lax.broadcasted_iota(jnp.int32, (every_x.shape[0], coarse_x), 1)
    ).astype(jnp.float32)
    tile_counts = jnp.dot(in_row, in_column, precision=HIGHEST, preferred_element_type=jnp.float32)
    cell_sums = jnp.einsum(
        "rj,jc,jk->rck", in_row, in_column, every_means, precision=HIGHEST
    )
    averaged = cell_sums / jnp.maximum(tile_counts, 1.0)[:, :, None]
    return (statistics, averaged.reshape(per_row, coarse_x * HW * 8))


def solution(mesh):
    in_specs = (P(None, None, "gx", "gy"), P(), P(), P())
    out_specs = (P(("gx", "gy"), None), P("gy", None))
    return jax.shard_map(shards, mesh=mesh, in_specs=in_specs, out_specs=out_specs, check_vma=False)
```

```python
import numpy as np
import jax
import jax.numpy as jnp
from jax import lax
from jax.sharding import PartitionSpec as P

TE = 16
HW = 4
CAP = 2


HIGHEST = lax.Precision.HIGHEST


def with_halo(block, sides, width):
    for axis, dim in sides:
        count = lax.axis_size(axis)
        forward = [(i, i + 1) for i in range(count - 1)]
        forward.append((count - 1, 0))
        backward = [(target, source) for source, target in forward]
        low = lax.ppermute(
            lax.slice_in_dim(block, block.shape[dim] - width, None, axis=dim), axis, forward
        )
        high = lax.ppermute(lax.slice_in_dim(block, 0, width, axis=dim), axis, backward)
        block = jnp.concatenate([low, block, high], axis=dim)
    return block


def band_matrix(half_width):
    span = TE + 2 * HW
    row_index = np.arange(TE)[:, None]
    column_index = np.arange(span)[None, :]
    inside = np.abs(column_index - row_index - HW) <= half_width
    return np.where(inside, np.float32(1.0 / (2 * half_width + 1)), np.float32(0.0)).astype(np.float32)


def plane_matrix(half_width):
    span = TE + 2 * HW
    weights = band_matrix(half_width).astype(np.float64)
    return np.einsum("ax,by->xyab", weights, weights).reshape(span * span, TE * TE).astype(np.float32)


def box_band(columns, half_width):
    along_z = jnp.einsum("az,qtzp->qtap", band_matrix(half_width), columns, precision=HIGHEST)
    return jnp.einsum("qtap,pc->qtac", along_z, plane_matrix(half_width), precision=HIGHEST)


def quantities(tiles):
    span = TE + 2 * HW
    tile_count = tiles.shape[0]
    cell_values = tiles.astype(jnp.float32).reshape(tile_count, tiles.shape[1], span, span * span)
    solid = cell_values[:, 0]
    gas_speed = [cell_values[:, 1 + direction] for direction in range(3)]
    grain_speed = [cell_values[:, 4 + direction] for direction in range(3)]
    pressure = cell_values[:, 7]
    granular = cell_values[:, 8]
    friction = cell_values[:, 9]
    quantity_list = [solid] + gas_speed + [pressure, friction]
    quantity_list = quantity_list + [solid * speed for speed in gas_speed]
    quantity_list = quantity_list + [solid * speed for speed in grain_speed]
    quantity_list = quantity_list + [solid * granular, solid * pressure]
    quantity_list = quantity_list + [
        friction * (gas_speed[direction] - grain_speed[direction]) for direction in range(3)
    ]
    return jnp.stack(quantity_list, axis=0)


def block_matrix():
    sub_edge = TE // 4
    plane_index = np.arange(TE * TE)[:, None]
    block_index = np.arange(sub_edge * sub_edge)[None, :]
    block_of = plane_index // TE // 4 * sub_edge + plane_index % TE // 4
    return np.where(block_of == block_index, np.float32(1.0 / 16.0), np.float32(0.0)).astype(np.float32)


def closure_blocks(smoothed):
    solid_mean = smoothed[0]
    components = []
    for direction in range(3):
        components.append(smoothed[6 + direction] / solid_mean - smoothed[1 + direction])
    for direction in range(3):
        components.append(
            smoothed[14 + direction]
            - smoothed[5] * (smoothed[6 + direction] - smoothed[9 + direction]) / solid_mean
        )
    components.append(smoothed[12] / solid_mean)
    components.append(smoothed[13] / solid_mean - smoothed[4])
    sub_edge = TE // 4
    tile_count = components[0].shape[0]
    depth_mean = jnp.stack(
        [
            jnp.mean(component.reshape(tile_count, sub_edge, 4, TE * TE), axis=2)
            for component in components
        ],
        axis=0,
    )
    blocks = jnp.einsum("ktzp,pc->ktzc", depth_mean, block_matrix(), precision=HIGHEST)
    return blocks.reshape(8, tile_count, sub_edge**3)


def tile_statistics(tiles):
    total_tiles = tiles.shape[0]
    columns = quantities(tiles)
    results = []
    for half_width in range(1, HW + 1):
        results.append(closure_blocks(box_band(columns, half_width)))
    mapped = jnp.stack(results, axis=0)
    return jnp.transpose(mapped, (2, 0, 1, 3)).reshape(total_tiles, HW * 8 * (TE // 4) ** 3)


def cut_tiles(padded, tile_ids, across_x, across_y):
    span = TE + 2 * HW
    depth_at = tile_ids // (across_x * across_y)
    column_at = tile_ids // across_y % across_x
    row_at = tile_ids % across_y
    pieces = []
    for index in range(tile_ids.shape[0]):
        window = lax.dynamic_slice(
            padded,
            (jnp.int32(0), depth_at[index] * TE, column_at[index] * TE, row_at[index] * TE),
            (padded.shape[0], span, span, span),
        )
        pieces.append(window.reshape(padded.shape[0], span * span * span))
    return jnp.stack(pieces, axis=0)


def shards(fields, dense_list, filter_device, pencil_order):
    groups_x = lax.axis_size("gx")
    groups_y = lax.axis_size("gy")
    self_column = lax.axis_index("gx")
    self_row = lax.axis_index("gy")
    across_x = fields.shape[2] // TE
    across_y = fields.shape[3] // TE
    list_length = dense_list.shape[2]
    per_filter = groups_x // 4 * (CAP + (CAP - 1) // 2)
    padded = with_halo(fields, (("gx", 2), ("gy", 3)), HW)
    padded = jnp.concatenate([padded[:, -HW:], padded, padded[:, :HW]], axis=1)
    own_tiles = dense_list[self_row, self_column]
    own_targets = filter_device[self_row, self_column]
    is_listed = own_targets >= 0
    before_mask = lax.broadcasted_iota(
        jnp.int32, (list_length, list_length), 0
    ) < lax.broadcasted_iota(jnp.int32, (list_length, list_length), 1)
    same_target = own_targets[:, None] == own_targets[None, :]
    send_rank = jnp.sum((same_target & before_mask).astype(jnp.int32), axis=0)
    send_slot = jnp.where(is_listed, own_targets * CAP + send_rank, groups_x * CAP)
    group_targets = filter_device[self_row]
    group_tiles = dense_list[self_row]
    arriving = (group_targets == self_column).astype(jnp.int32)
    row_rank = jnp.cumsum(arriving, axis=1) - arriving
    source_no = lax.broadcasted_iota(jnp.int32, (groups_x, list_length), 0)
    arrival_slot = (source_no * CAP + row_rank).reshape(-1)
    arrival_order = jnp.cumsum(arriving.reshape(-1)) - 1
    arrival_pos = jnp.where(arriving.reshape(-1) > 0, arrival_order, per_filter)
    take_slot = jnp.zeros((per_filter,), jnp.int32).at[arrival_pos].set(arrival_slot, mode="drop")
    take_tile = (
        jnp.zeros((per_filter,), jnp.int32)
        .at[arrival_pos]
        .set(group_tiles.reshape(-1), mode="drop")
    )
    take_source = (
        jnp.zeros((per_filter,), jnp.int32).at[arrival_pos].set(source_no.reshape(-1), mode="drop")
    )
    own_cut = cut_tiles(padded, jnp.where(is_listed, own_tiles, 0), across_x, across_y)
    own_statistics = tile_statistics(own_cut)
    stat_length = own_statistics.shape[1]
    outgoing = (
        jnp.zeros((groups_x * CAP, stat_length), jnp.float32)
        .at[send_slot]
        .set(own_statistics, mode="drop")
        .reshape(groups_x, CAP, stat_length)
    )
    incoming = lax.all_to_all(outgoing, "gx", split_axis=0, concat_axis=0, tiled=True)
    statistics = incoming.reshape(groups_x * CAP, stat_length)[take_slot]
    own_means = jnp.where(
        is_listed[:, None],
        jnp.mean(own_statistics.reshape(list_length, HW * 8, stat_length // (HW * 8)), axis=2),
        0.0,
    )
    every_means = lax.all_gather(
        lax.all_gather(own_means, "gy", axis=0, tiled=False), "gx", axis=0, tiled=False
    )
    every_means = jnp.transpose(
        every_means.reshape(groups_x, groups_y, list_length, HW * 8), (1, 0, 2, 3)
    ).reshape(groups_y * groups_x * list_length, HW * 8)
    pencils = pencil_order.shape[0]
    coarse_x = across_x * groups_x // 2
    per_row = pencils // groups_y
    row_pencils = lax.dynamic_slice_in_dim(pencil_order, self_row * per_row, per_row)
    every_tile = dense_list.reshape(-1)
    every_valid = every_tile >= 0
    every_group = lax.broadcasted_iota(jnp.int32, dense_list.shape, 0).reshape(-1)
    every_source = lax.broadcasted_iota(jnp.int32, dense_list.shape, 1).reshape(-1)
    every_y = (every_group * across_y + every_tile % across_y) // 2
    every_x = (every_source * across_x + every_tile // across_y % across_x) // 2
    in_row = ((row_pencils[:, None] == every_y[None, :]) & every_valid[None, :]).astype(jnp.float32)
    in_column = (
        every_x[:, None] == lax.broadcasted_iota(jnp.int32, (every_x.shape[0], coarse_x), 1)
    ).astype(jnp.float32)
    tile_counts = jnp.dot(in_row, in_column, precision=HIGHEST, preferred_element_type=jnp.float32)
    cell_sums = jnp.einsum(
        "rj,jc,jk->rck", in_row, in_column, every_means, precision=HIGHEST
    )
    averaged = cell_sums / jnp.maximum(tile_counts, 1.0)[:, :, None]
    return (statistics, averaged.reshape(per_row, coarse_x * HW * 8))


def solution(mesh):
    in_specs = (P(None, None, "gx", "gy"), P(), P(), P())
    out_specs = (P(("gx", "gy"), None), P("gy", None))
    return jax.shard_map(shards, mesh=mesh, in_specs=in_specs, out_specs=out_specs, check_vma=False)
```
